1024 devices in a mesh: section: 32 (over x, y), ctx: 32 (over z, core).
Axes of the slice: x: 4, y: 8, z: 16, core: 2. Of those that a mesh axis runs over, the one named last changes fastest.
Arguments:
- queries: bfloat16 [32, 8192, 1024], P('section', 'ctx'), may hold values from -2.5 to 2.5
- attn_keys: bfloat16 [32, 8192, 128], P('section', 'ctx'), may hold values from -2.5 to 2.5
- attn_values: bfloat16 [32, 8192, 128], P('section', 'ctx'), may hold values from -4 to 4
- attn_outputs: bfloat16 [32, 8192, 1024], P('section', 'ctx'), may hold values from -4 to 4
- head_grad: bfloat16 [32, 8192, 1024], P('section', 'ctx'), may hold values from -4 to 4
- next_grad: bfloat16 [32, 8192, 1024], P('section', 'ctx'), may hold values from -4 to 4
- lse_saved: float32 [32, 8, 8192], P('section', None, 'ctx'), may hold values from 4 to 7
- block_keys: int32 [64, 7], P('ctx'), may hold values from -1 to 63, as said below
Outputs:
- query_grads: bfloat16 [32, 8192, 1024], P('section', 'ctx')
- key_grads: bfloat16 [32, 8192, 128], P('section', 'ctx')
- value_grads: bfloat16 [32, 8192, 128], P('section', 'ctx')
The draws below stay inside these ranges and needn't reach their ends.
Inputs may be any that keep to these rules, and one draw needn't show every extreme that they name: `block_keys`: row i lists distinct blocks, none after block i: first its window i, i - 1, ..., i - w + 1 for some w of 1 to 4, then, falling, every block j before the window with j % 16 == 15; the remaining slots hold -1. The last row's window has 4 blocks.
All inputs are finite; a program needn't handle non-finite values.
Results may differ from the reference program's by a relative error of at most 0.018.
Values may be sent and summed in bfloat16 or wider, within the bound.
No kernel may reach another device: no remote copies, remote signals or barrier semaphores. Data moves between devices by JAX's collectives and lax.ppermute only.
A program may use at most 64 MiB of HBM per device.

```python
import jax
import jax.numpy as jnp
from jax import lax

HEAD = 128
GROUP = 8
BLK = 128
WIN = 4
BLK_DEV = 2
SECTIONS = 32
BLOCKS = 64
SEQ = 8192
STRIDE = 16
MAXK = 7
WIDTH = 1024
N_CTX = 32


def draw_block_keys(key, part):
    row_ids = jnp.arange(BLOCKS, dtype=jnp.int32)
    widths = jax.random.randint(key, (BLOCKS,), 1, WIN + 1, dtype=jnp.int32)
    widths = jnp.where(row_ids == BLOCKS - 1, WIN, widths)
    widths = jnp.minimum(widths, row_ids + 1)
    slot_ids = jnp.arange(MAXK, dtype=jnp.int32)
    window = row_ids[:, None] - slot_ids[None, :]
    earlier = (row_ids - widths + 1) // STRIDE
    rank_back = earlier[:, None] - 1 - (slot_ids[None, :] - widths[:, None])
    summary = rank_back * STRIDE + STRIDE - 1
    listed = jnp.where(slot_ids[None, :] < widths[:, None], window, jnp.where(rank_back >= 0, summary, -1))
    return listed.astype(jnp.int32)


def block_levels(key, shape, split, smallest, largest):
    gain = 1.0
    for position, blocks in split:
        steps = jax.random.uniform(jax.random.fold_in(jax.random.fold_in(key, 6), position), (blocks,), jnp.float32, smallest / len(split), largest / len(split))
        gain = gain * jnp.repeat(jnp.exp(steps), shape[position] // blocks).reshape((-1,) + (1,) * (len(shape) - 1 - position))
    return gain


def gaussian(stream_key, shape, scale, bound, shards=(), kind=jnp.bfloat16):
    gain = block_levels(stream_key, shape, shards, -0.22, 0.18) if shards else 1.0
    values = jax.random.normal(stream_key, shape, jnp.float32) * scale * gain
    return jnp.minimum(jnp.maximum(values, -bound), bound).astype(kind)


def setup_inputs(seed: int = 0) -> dict:
    key_list = jax.random.split(jax.random.key(seed), 9)
    return {
        "queries": gaussian(key_list[0], (SECTIONS, SEQ, WIDTH), 1.0, 2.5, ((0, 32), (1, 32))),
        "attn_keys": gaussian(key_list[1], (SECTIONS, SEQ, HEAD), 1.0, 2.5, ((0, 32), (1, 32))),
        "attn_values": gaussian(key_list[2], (SECTIONS, SEQ, HEAD), 1.0, 4.0, ((0, 32), (1, 32))),
        "attn_outputs": gaussian(key_list[3], (SECTIONS, SEQ, WIDTH), 1.0, 4.0, ((0, 32), (1, 32))),
        "head_grad": gaussian(key_list[4], (SECTIONS, SEQ, WIDTH), 1.0, 4.0, ((0, 32), (1, 32))),
        "next_grad": gaussian(key_list[5], (SECTIONS, SEQ, WIDTH), 1.0, 4.0, ((0, 32), (1, 32))),
        "lse_saved": jnp.clip(4.0 + 3.0 * jax.random.uniform(key_list[6], (SECTIONS, GROUP, SEQ), jnp.float32) ** block_levels(key_list[6], (SECTIONS, GROUP, SEQ), ((0, 32), (2, 32)), -0.2, 0.2), 4.0, 7.0),
        "block_keys": draw_block_keys(jax.random.fold_in(key_list[8], 71), 0),
    }


def section_grads(queries, attn_keys, attn_values, upstream, lse_rows, deltas, block_keys):
    score_scale = HEAD ** -0.5
    positions = jnp.arange(BLK, dtype=jnp.int32)
    causal = positions[None, :] <= positions[:, None]
    query_heads = queries.reshape(SEQ, GROUP, HEAD).astype(jnp.float32)
    upstream_heads = upstream.reshape(SEQ, GROUP, HEAD).astype(jnp.float32)
    key_rows = attn_keys.astype(jnp.float32)
    value_rows = attn_values.astype(jnp.float32)

    def one_block(partial_value, block_index):
        row_start = (block_index * BLK).astype(jnp.int32)
        query_block = lax.dynamic_slice_in_dim(query_heads, row_start, BLK, 0)
        upstream_block = lax.dynamic_slice_in_dim(upstream_heads, row_start, BLK, 0)
        lse_block = lax.dynamic_slice_in_dim(lse_rows, row_start, BLK, 1)
        delta_block = lax.dynamic_slice_in_dim(deltas, row_start, BLK, 1)
        row_keys = block_keys[block_index]

        def one_slot(slot_state, target):
            grad_q, partial_value = slot_state
            usable = target >= 0
            safe_target = jnp.maximum(target, 0).astype(jnp.int32)
            key_start = (safe_target * BLK).astype(jnp.int32)
            key_tile = lax.dynamic_slice_in_dim(key_rows, key_start, BLK, 0)
            value_tile = lax.dynamic_slice_in_dim(value_rows, key_start, BLK, 0)
            scores = jnp.einsum("tgh,uh->gtu", query_block, key_tile) * score_scale
            allowed = usable & ((target < block_index) | causal)
            weights = jnp.where(allowed[None], jnp.exp(scores - lse_block[:, :, None]), 0.0)
            dweights = jnp.einsum("tgh,uh->gtu", upstream_block, value_tile)
            dscores = weights * (dweights - delta_block[:, :, None])
            weights_low = lax.optimization_barrier(weights.astype(jnp.bfloat16)).astype(jnp.float32)
            dscores_low = lax.optimization_barrier(dscores.astype(jnp.bfloat16)).astype(jnp.float32)
            grad_q = grad_q + jnp.einsum("gtu,uh->tgh", dscores_low, key_tile)
            key_part = jnp.einsum("gtu,tgh->uh", dscores_low, query_block) * score_scale
            value_part = jnp.einsum("gtu,tgh->uh", weights_low, upstream_block)
            previous = lax.dynamic_slice_in_dim(partial_value, key_start, BLK, 0)
            update = previous + jnp.concatenate([key_part, value_part], axis=1)
            partial_value = lax.dynamic_update_slice_in_dim(partial_value, update, key_start, 0)
            return (grad_q, partial_value), None

        start_state = (jnp.zeros((BLK, GROUP, HEAD), jnp.float32), partial_value)
        (grad_q, partial_value), unused = lax.scan(one_slot, start_state, row_keys)
        block_grads = (grad_q * score_scale).reshape(BLK, GROUP * HEAD).astype(jnp.bfloat16)
        return partial_value, block_grads

    def one_group(totals, group_index):
        blocks_here = (group_index * BLK_DEV + jnp.arange(BLK_DEV, dtype=jnp.int32)).astype(jnp.int32)
        partial_value, block_grads = lax.scan(one_block, jnp.zeros((SEQ, 2 * HEAD), jnp.float32), blocks_here)
        rounded = lax.optimization_barrier(partial_value.astype(jnp.bfloat16)).astype(jnp.float32)
        return totals + rounded, block_grads

    totals, group_grads = lax.scan(one_group, jnp.zeros((SEQ, 2 * HEAD), jnp.float32), jnp.arange(N_CTX, dtype=jnp.int32))
    query_grads = group_grads.reshape(SEQ, GROUP * HEAD)
    return query_grads, totals[:, :HEAD].astype(jnp.bfloat16), totals[:, HEAD:].astype(jnp.bfloat16)


def reference(queries, attn_keys, attn_values, attn_outputs, head_grad, next_grad, lse_saved, block_keys):
    incoming = jnp.concatenate([next_grad[1:], jnp.zeros_like(next_grad[:1])], axis=0)
    upstream = (head_grad.astype(jnp.float32) + incoming.astype(jnp.float32)).astype(jnp.bfloat16)
    products = upstream.astype(jnp.float32) * attn_outputs.astype(jnp.float32)
    deltas = jnp.swapaxes(products.reshape(SECTIONS, SEQ, GROUP, HEAD).sum(axis=3), 1, 2)

    def per_section(section_items):
        section_queries, section_keys, section_values, section_upstream, section_lse, section_deltas = section_items
        return section_grads(section_queries, section_keys, section_values, section_upstream, section_lse, section_deltas, block_keys)

    query_grads, key_grads, value_grads = lax.map(per_section, (queries, attn_keys, attn_values, upstream, lse_saved, deltas))
    return (query_grads, key_grads, value_grads)
```

```python
import jax
import jax.numpy as jnp
from jax import lax
from jax.sharding import PartitionSpec as P

SUMMARY = 4
WINDOW = 4


def from_behind(block, axis, distance):
    devices = range(lax.axis_size(axis))
    route = [(i - distance, i) for i in devices if i - distance in devices]
    return lax.ppermute(block, axis, route)


def on_device(
    queries, attn_keys, attn_values, attn_outputs, head_grad, next_grad, lse_saved, block_keys
):
    tokens = queries.shape[1]
    features = queries.shape[2]
    head_size = attn_keys.shape[2]
    group_heads = features // head_size
    local_blocks = block_keys.shape[0]
    block_rows = tokens // local_blocks
    score_scale = head_size ** (-0.5)
    ctx_count = lax.axis_size("ctx")
    blocks = local_blocks * ctx_count
    stride = blocks // SUMMARY
    reach = WINDOW - 1
    behind = -(-reach // local_blocks)
    counts = [min(local_blocks, reach - (k - 1) * local_blocks) for k in range(1, behind + 1)]
    span = reach + local_blocks
    n_summary = blocks // stride - 1
    device = lax.axis_index("ctx")
    first_block = device * local_blocks
    low_block = first_block - reach

    incoming = from_behind(next_grad, "section", -1)
    upstream = (head_grad[0].astype(jnp.float32) + incoming[0].astype(jnp.float32)).astype(
        jnp.bfloat16
    )
    products = upstream.astype(jnp.float32) * attn_outputs[0].astype(jnp.float32)
    deltas = jnp.sum(products.reshape(local_blocks, block_rows, group_heads, head_size), axis=3)
    deltas = jnp.swapaxes(deltas, 1, 2)
    lse_rows = jnp.swapaxes(lse_saved[0].reshape(group_heads, local_blocks, block_rows), 0, 1)

    paired = jnp.concatenate([attn_keys[0], attn_values[0]], axis=1)
    pieces = []
    for k in range(behind, 0, -1):
        piece = paired[(local_blocks - counts[k - 1]) * block_rows :]
        pieces.append(from_behind(piece, "ctx", k))
    pieces.append(paired)
    own_blocks = paired.reshape(local_blocks, block_rows, 2 * head_size)
    summary_parts = []
    for k in range(n_summary):
        summary_block = k * stride + stride - 1
        owner = summary_block // local_blocks
        summary_parts.append(
            jnp.where(device == owner, own_blocks[summary_block % local_blocks], 0).astype(
                jnp.bfloat16
            )
        )
    summary_kv = lax.psum(jnp.stack(summary_parts), "ctx")
    table = jnp.concatenate(pieces + [summary_kv.reshape(n_summary * block_rows, -1)], axis=0)
    key_table = table[:, :head_size]
    value_table = table[:, head_size:]
    slots = span + n_summary

    targets = block_keys
    slot_of = jnp.where(targets >= low_block, targets - low_block, span + targets // stride)
    slot_of = jnp.where(targets >= 0, slot_of, -1)
    chosen = jnp.any(slot_of[:, :, None] == jnp.arange(slots)[None, None, :], axis=1)
    table_ids = jnp.concatenate(
        [
            low_block + jnp.arange(span, dtype=jnp.int32),
            jnp.arange(n_summary, dtype=jnp.int32) * stride + stride - 1,
        ]
    )
    query_ids = first_block + jnp.arange(local_blocks, dtype=jnp.int32)
    positions = jnp.arange(block_rows, dtype=jnp.int32)
    causal = positions[None, :] <= positions[:, None]
    earlier = table_ids[None, :] < query_ids[:, None]
    allowed = chosen[:, None, :, None] & (earlier[:, None, :, None] | causal[None, :, None, :])
    allowed = allowed.reshape(local_blocks, block_rows, slots * block_rows)

    query_heads = queries[0].reshape(local_blocks, block_rows, group_heads, head_size)
    upstream_heads = upstream.reshape(local_blocks, block_rows, group_heads, head_size)
    scores = (
        jnp.einsum("rtgh,uh->rgtu", query_heads, key_table, preferred_element_type=jnp.float32)
        * score_scale
    )
    weights = jnp.where(allowed[:, None], jnp.exp(scores - lse_rows[:, :, :, None]), 0.0)
    dweights = jnp.einsum(
        "rtgh,uh->rgtu", upstream_heads, value_table, preferred_element_type=jnp.float32
    )
    dscores = weights * (dweights - deltas[:, :, :, None])
    weights_low = weights.astype(jnp.bfloat16)
    dscores_low = dscores.astype(jnp.bfloat16)
    grad_q = jnp.einsum("rgtu,uh->rtgh", dscores_low, key_table, preferred_element_type=jnp.float32)
    query_grads = (grad_q * score_scale).reshape(tokens, features).astype(jnp.bfloat16)
    key_part = (
        jnp.einsum("rgtu,rtgh->uh", dscores_low, query_heads, preferred_element_type=jnp.float32)
        * score_scale
    )
    value_part = jnp.einsum(
        "rgtu,rtgh->uh", weights_low, upstream_heads, preferred_element_type=jnp.float32
    )
    partial = jnp.concatenate([key_part, value_part], axis=1).astype(jnp.bfloat16)

    totals = partial[(span - local_blocks) * block_rows : span * block_rows].astype(jnp.float32)
    offset = 0
    for k in range(behind, 0, -1):
        size = counts[k - 1] * block_rows
        returned = from_behind(partial[offset : offset + size], "ctx", -k).astype(jnp.float32)
        totals = totals.at[tokens - size :].add(returned)
        offset += size
    summary_grads = lax.psum(
        partial[span * block_rows :].astype(jnp.float32).reshape(n_summary, block_rows, -1), "ctx"
    )
    for k in range(n_summary):
        summary_block = k * stride + stride - 1
        owner = summary_block // local_blocks
        start = (summary_block % local_blocks) * block_rows
        mine = jnp.where(device == owner, summary_grads[k], 0.0)
        totals = totals.at[start : start + block_rows].add(mine)
    key_grads = totals[:, :head_size].astype(jnp.bfloat16)
    value_grads = totals[:, head_size:].astype(jnp.bfloat16)
    return (query_grads[None], key_grads[None], value_grads[None])


def solution(mesh):
    placed = (
        P("section", "ctx", None),
        P("section", "ctx", None),
        P("section", "ctx", None),
        P("section", "ctx", None),
        P("section", "ctx", None),
        P("section", "ctx", None),
        P("section", None, "ctx"),
        P("ctx", None),
    )
    return jax.shard_map(
        on_device,
        mesh=mesh,
        in_specs=placed,
        out_specs=(P("section", "ctx", None), P("section", "ctx", None), P("section", "ctx", None)),
        check_vma=False,
    )
```

```python
import jax
import jax.numpy as jnp
from jax import lax
from jax.sharding import PartitionSpec as P

SUMMARY = 4
WINDOW = 4


def from_behind(block, axis, distance):
    devices = range(lax.axis_size(axis))
    route = [(i - distance, i) for i in devices if i - distance in devices]
    return lax.ppermute(block, axis, route)


def on_device(
    queries, attn_keys, attn_values, attn_outputs, head_grad, next_grad, lse_saved, block_keys
):
    tokens = queries.shape[1]
    features = queries.shape[2]
    head_size = attn_keys.shape[2]
    group_heads = features // head_size
    local_blocks = block_keys.shape[0]
    block_rows = tokens // local_blocks
    score_scale = head_size ** (-0.5)
    ctx_count = lax.axis_size("ctx")
    blocks = local_blocks * ctx_count
    stride = blocks // SUMMARY
    reach = WINDOW - 1
    behind = -(-reach // local_blocks)
    counts = [min(local_blocks, reach - (k - 1) * local_blocks) for k in range(1, behind + 1)]
    span = reach + local_blocks
    n_summary = blocks // stride - 1
    device = lax.axis_index("ctx")
    first_block = device * local_blocks
    low_block = first_block - reach

    incoming = from_behind(next_grad, "section", -1)
    upstream = (head_grad[0].astype(jnp.float32) + incoming[0].astype(jnp.float32)).astype(
        jnp.bfloat16
    )
    products = upstream.astype(jnp.float32) * attn_outputs[0].astype(jnp.float32)
    deltas = jnp.sum(products.reshape(local_blocks, block_rows, group_heads, head_size), axis=3)
    deltas = jnp.swapaxes(deltas, 1, 2)
    lse_rows = jnp.swapaxes(lse_saved[0].reshape(group_heads, local_blocks, block_rows), 0, 1)

    paired = jnp.concatenate([attn_keys[0], attn_values[0]], axis=1)
    pieces = []
    for k in range(behind, 0, -1):
        piece = paired[(local_blocks - counts[k - 1]) * block_rows :]
        pieces.append(from_behind(piece, "ctx", k))
    pieces.append(paired)
    own_blocks = paired.reshape(local_blocks, block_rows, 2 * head_size)
    owners = [(k * stride + stride - 1) // local_blocks for k in range(n_summary)]
    owned = own_blocks[(stride - 1) % local_blocks]
    radix = 1
    while radix * radix < ctx_count:
        radix += 1
    relay_of = [-1] * ctx_count
    for k, owner in enumerate(owners):
        for x in range(owner, min(owner + radix, ctx_count)):
            relay_of[x] = k
    relay_table = jnp.array(relay_of, dtype=jnp.int32)
    is_owner = jnp.array([x in owners for x in range(ctx_count)])[device]
    held = jnp.where(is_owner, owned, 0).astype(jnp.bfloat16)
    for shift in range(1, radix):
        route = [(o, o + shift) for o in owners if o + shift < ctx_count]
        held = held + lax.ppermute(owned, "ctx", route)
    summary_parts = [jnp.where(relay_table[device] == k, held, 0) for k in range(n_summary)]
    for hop in range(1, radix):
        shift = hop * radix
        route = [(x, x + shift) for x in range(ctx_count - shift) if relay_of[x] >= 0]
        arrived = lax.ppermute(held, "ctx", route)
        for k in range(n_summary):
            came = [x + shift < ctx_count and relay_of[x] == k for x in range(ctx_count)]
            came = jnp.array([False] * shift + came[: ctx_count - shift])
            summary_parts[k] = summary_parts[k] + jnp.where(came[device], arrived, 0)
    summary_kv = jnp.stack(summary_parts).astype(jnp.bfloat16)
    table = jnp.concatenate(pieces + [summary_kv.reshape(n_summary * block_rows, -1)], axis=0)
    key_table = table[:, :head_size]
    value_table = table[:, head_size:]
    slots = span + n_summary

    targets = block_keys
    slot_of = jnp.where(targets >= low_block, targets - low_block, span + targets // stride)
    slot_of = jnp.where(targets >= 0, slot_of, -1)
    chosen = jnp.any(slot_of[:, :, None] == jnp.arange(slots)[None, None, :], axis=1)
    table_ids = jnp.concatenate(
        [
            low_block + jnp.arange(span, dtype=jnp.int32),
            jnp.arange(n_summary, dtype=jnp.int32) * stride + stride - 1,
        ]
    )
    query_ids = first_block + jnp.arange(local_blocks, dtype=jnp.int32)
    positions = jnp.arange(block_rows, dtype=jnp.int32)
    causal = positions[None, :] <= positions[:, None]
    earlier = table_ids[None, :] < query_ids[:, None]
    allowed = chosen[:, None, :, None] & (earlier[:, None, :, None] | causal[None, :, None, :])
    allowed = allowed.reshape(local_blocks, block_rows, slots * block_rows)

    query_heads = queries[0].reshape(local_blocks, block_rows, group_heads, head_size)
    upstream_heads = upstream.reshape(local_blocks, block_rows, group_heads, head_size)
    scores = (
        jnp.einsum("rtgh,uh->rgtu", query_heads, key_table, preferred_element_type=jnp.float32)
        * score_scale
    )
    weights = jnp.where(allowed[:, None], jnp.exp(scores - lse_rows[:, :, :, None]), 0.0)
    dweights = jnp.einsum(
        "rtgh,uh->rgtu", upstream_heads, value_table, preferred_element_type=jnp.float32
    )
    dscores = weights * (dweights - deltas[:, :, :, None])
    weights_low = weights.astype(jnp.bfloat16)
    dscores_low = dscores.astype(jnp.bfloat16)
    grad_q = jnp.einsum("rgtu,uh->rtgh", dscores_low, key_table, preferred_element_type=jnp.float32)
    query_grads = (grad_q * score_scale).reshape(tokens, features).astype(jnp.bfloat16)
    key_part = (
        jnp.einsum("rgtu,rtgh->uh", dscores_low, query_heads, preferred_element_type=jnp.float32)
        * score_scale
    )
    value_part = jnp.einsum(
        "rgtu,rtgh->uh", weights_low, upstream_heads, preferred_element_type=jnp.float32
    )
    partial = jnp.concatenate([key_part, value_part], axis=1).astype(jnp.bfloat16)

    totals = partial[(span - local_blocks) * block_rows : span * block_rows].astype(jnp.float32)
    offset = 0
    for k in range(behind, 0, -1):
        size = counts[k - 1] * block_rows
        returned = from_behind(partial[offset : offset + size], "ctx", -k).astype(jnp.float32)
        totals = totals.at[tokens - size :].add(returned)
        offset += size
    summary_low = partial[span * block_rows :].reshape(n_summary, block_rows, -1)
    tree_slot = jnp.maximum(relay_table[device], 0)
    gathered = lax.dynamic_index_in_dim(summary_low, tree_slot, 0, keepdims=False).astype(
        jnp.float32
    )
    for hop in range(1, radix):
        shift = hop * radix
        route = [(x + shift, x) for x in range(ctx_count - shift) if relay_of[x] >= 0]
        sent_slot = [max(relay_of[y - shift], 0) if y >= shift else 0 for y in range(ctx_count)]
        slot_here = jnp.array(sent_slot, dtype=jnp.int32)[device]
        outgoing = lax.dynamic_index_in_dim(summary_low, slot_here, 0, keepdims=False)
        gathered = gathered + lax.ppermute(outgoing, "ctx", route).astype(jnp.float32)
    owner_total = gathered
    for shift in range(1, radix):
        route = [(o + shift, o) for o in owners if o + shift < ctx_count]
        owner_total = owner_total + lax.ppermute(gathered, "ctx", route)
    start = ((stride - 1) % local_blocks) * block_rows
    mine = jnp.where(is_owner, owner_total, 0.0)
    totals = totals.at[start : start + block_rows].add(mine)
    key_grads = totals[:, :head_size].astype(jnp.bfloat16)
    value_grads = totals[:, head_size:].astype(jnp.bfloat16)
    return (query_grads[None], key_grads[None], value_grads[None])


def solution(mesh):
    placed = (
        P("section", "ctx", None),
        P("section", "ctx", None),
        P("section", "ctx", None),
        P("section", "ctx", None),
        P("section", "ctx", None),
        P("section", "ctx", None),
        P("section", None, "ctx"),
        P("ctx", None),
    )
    return jax.shard_map(
        on_device,
        mesh=mesh,
        in_specs=placed,
        out_specs=(P("section", "ctx", None), P("section", "ctx", None), P("section", "ctx", None)),
        check_vma=False,
    )
```

```python
import functools

import jax
import jax.numpy as jnp
from jax import lax
from jax.sharding import PartitionSpec as P

SUMMARY = 4
WINDOW = 4


def from_behind(block, axis, distance):
    devices = range(lax.axis_size(axis))
    route = [(i - distance, i) for i in devices if i - distance in devices]
    return lax.ppermute(block, axis, route)


def on_device(
    queries, attn_keys, attn_values, attn_outputs, head_grad, next_grad, lse_saved, block_keys
):
    tokens = queries.shape[1]
    features = queries.shape[2]
    head_size = attn_keys.shape[2]
    group_heads = features // head_size
    local_blocks = block_keys.shape[0]
    block_rows = tokens // local_blocks
    score_scale = head_size ** (-0.5)
    ctx_count = lax.axis_size("ctx")
    blocks = local_blocks * ctx_count
    stride = blocks // SUMMARY
    reach = WINDOW - 1
    behind = -(-reach // local_blocks)
    counts = [min(local_blocks, reach - (k - 1) * local_blocks) for k in range(1, behind + 1)]
    span = reach + local_blocks
    n_summary = blocks // stride - 1
    device = lax.axis_index("ctx")
    first_block = device * local_blocks
    low_block = first_block - reach

    incoming = from_behind(next_grad, "section", -1)
    upstream = (head_grad[0].astype(jnp.float32) + incoming[0].astype(jnp.float32)).astype(
        jnp.bfloat16
    )
    products = upstream.astype(jnp.float32) * attn_outputs[0].astype(jnp.float32)
    deltas = jnp.sum(products.reshape(local_blocks, block_rows, group_heads, head_size), axis=3)
    deltas = jnp.swapaxes(deltas, 1, 2)
    lse_rows = jnp.swapaxes(lse_saved[0].reshape(group_heads, local_blocks, block_rows), 0, 1)

    paired = jnp.concatenate([attn_keys[0], attn_values[0]], axis=1)
    own_blocks = paired.reshape(local_blocks, block_rows, 2 * head_size)
    owners = [(k * stride + stride - 1) // local_blocks for k in range(n_summary)]
    radix = 1
    while radix * radix < ctx_count - owners[0]:
        radix += 1

    def member(position, k):
        return (position >= owners[k]) & (position < owners[k] + radix)

    relays = [x for x in range(ctx_count) if any(o <= x < o + radix for o in owners)]
    is_owner = functools.reduce(jnp.logical_or, [device == o for o in owners])
    owned = jnp.where(is_owner, own_blocks[(stride - 1) % local_blocks], 0).astype(jnp.bfloat16)
    held = owned
    pieces = []
    for k in range(behind, 0, -1):
        size = counts[k - 1] * block_rows
        piece = paired[tokens - size :]
        if k < radix:
            arrived = from_behind(jnp.concatenate([piece, owned], axis=0), "ctx", k)
            pieces.append(arrived[:size])
            held = held + arrived[size:]
        else:
            pieces.append(from_behind(piece, "ctx", k))
    pieces.append(paired)
    for shift in range(behind + 1, radix):
        route = [(o, o + shift) for o in owners if o + shift < ctx_count]
        held = held + lax.ppermute(owned, "ctx", route)
    summary_parts = [jnp.where(member(device, k), held, 0) for k in range(n_summary)]
    for hop in range(1, radix):
        shift = hop * radix
        route = [(x, x + shift) for x in relays if x + shift < ctx_count]
        arrived = lax.ppermute(held, "ctx", route)
        for k in range(n_summary):
            summary_parts[k] = summary_parts[k] + jnp.where(member(device - shift, k), arrived, 0)
    summary_kv = jnp.stack(summary_parts).astype(jnp.bfloat16)
    table = jnp.concatenate(pieces + [summary_kv.reshape(n_summary * block_rows, -1)], axis=0)
    key_table = table[:, :head_size]
    value_table = table[:, head_size:]
    slots = span + n_summary

    targets = block_keys
    slot_of = jnp.where(targets >= low_block, targets - low_block, span + targets // stride)
    slot_of = jnp.where(targets >= 0, slot_of, -1)
    chosen = jnp.any(slot_of[:, :, None] == jnp.arange(slots)[None, None, :], axis=1)
    table_ids = jnp.concatenate(
        [
            low_block + jnp.arange(span, dtype=jnp.int32),
            jnp.arange(n_summary, dtype=jnp.int32) * stride + stride - 1,
        ]
    )
    query_ids = first_block + jnp.arange(local_blocks, dtype=jnp.int32)
    positions = jnp.arange(block_rows, dtype=jnp.int32)
    causal = positions[None, :] <= positions[:, None]
    earlier = table_ids[None, :] < query_ids[:, None]
    allowed = chosen[:, None, :, None] & (earlier[:, None, :, None] | causal[None, :, None, :])
    allowed = allowed.reshape(local_blocks, block_rows, slots * block_rows)

    query_heads = queries[0].reshape(local_blocks, block_rows, group_heads, head_size)
    upstream_heads = upstream.reshape(local_blocks, block_rows, group_heads, head_size)
    scores = (
        jnp.einsum("rtgh,uh->rgtu", query_heads, key_table, preferred_element_type=jnp.float32)
        * score_scale
    )
    weights = jnp.where(allowed[:, None], jnp.exp(scores - lse_rows[:, :, :, None]), 0.0)
    dweights = jnp.einsum(
        "rtgh,uh->rgtu", upstream_heads, value_table, preferred_element_type=jnp.float32
    )
    dscores = weights * (dweights - deltas[:, :, :, None])
    weights_low = weights.astype(jnp.bfloat16)
    dscores_low = dscores.astype(jnp.bfloat16)
    grad_q = jnp.einsum("rgtu,uh->rtgh", dscores_low, key_table, preferred_element_type=jnp.float32)
    query_grads = (grad_q * score_scale).reshape(tokens, features).astype(jnp.bfloat16)
    key_part = (
        jnp.einsum("rgtu,rtgh->uh", dscores_low, query_heads, preferred_element_type=jnp.float32)
        * score_scale
    )
    value_part = jnp.einsum(
        "rgtu,rtgh->uh", weights_low, upstream_heads, preferred_element_type=jnp.float32
    )
    partial = jnp.concatenate([key_part, value_part], axis=1).astype(jnp.bfloat16)

    totals = partial[(span - local_blocks) * block_rows : span * block_rows].astype(jnp.float32)
    offset = 0
    for k in range(behind, 0, -1):
        size = counts[k - 1] * block_rows
        returned = from_behind(partial[offset : offset + size], "ctx", -k).astype(jnp.float32)
        totals = totals.at[tokens - size :].add(returned)
        offset += size
    summary_low = partial[span * block_rows :].reshape(n_summary, block_rows, -1)

    def slot_at(position):
        return sum(jnp.where(member(position, k), k, 0) for k in range(n_summary))

    gathered = lax.dynamic_index_in_dim(summary_low, slot_at(device), 0, keepdims=False)
    gathered = gathered.astype(jnp.float32)
    for hop in range(1, radix):
        shift = hop * radix
        route = [(x + shift, x) for x in relays if x + shift < ctx_count]
        outgoing = lax.dynamic_index_in_dim(summary_low, slot_at(device - shift), 0, keepdims=False)
        gathered = gathered + lax.ppermute(outgoing, "ctx", route).astype(jnp.float32)
    owner_total = gathered
    for shift in range(1, radix):
        route = [(o + shift, o) for o in owners if o + shift < ctx_count]
        owner_total = owner_total + lax.ppermute(gathered, "ctx", route)
    start = ((stride - 1) % local_blocks) * block_rows
    mine = jnp.where(is_owner, owner_total, 0.0)
    totals = totals.at[start : start + block_rows].add(mine)
    key_grads = totals[:, :head_size].astype(jnp.bfloat16)
    value_grads = totals[:, head_size:].astype(jnp.bfloat16)
    return (query_grads[None], key_grads[None], value_grads[None])


def solution(mesh):
    placed = (
        P("section", "ctx", None),
        P("section", "ctx", None),
        P("section", "ctx", None),
        P("section", "ctx", None),
        P("section", "ctx", None),
        P("section", "ctx", None),
        P("section", None, "ctx"),
        P("ctx", None),
    )
    return jax.shard_map(
        on_device,
        mesh=mesh,
        in_specs=placed,
        out_specs=(P("section", "ctx", None), P("section", "ctx", None), P("section", "ctx", None)),
        check_vma=False,
    )
```

```python
import functools

import jax
import jax.numpy as jnp
from jax import lax
from jax.sharding import PartitionSpec as P

SUMMARY = 4
WINDOW = 4


def from_behind(block, axis, distance):
    devices = range(lax.axis_size(axis))
    route = [(i - distance, i) for i in devices if i - distance in devices]
    return lax.ppermute(block, axis, route)


def on_device(
    queries, attn_keys, attn_values, attn_outputs, head_grad, next_grad, lse_saved, block_keys
):
    tokens = queries.shape[1]
    features = queries.shape[2]
    head_size = attn_keys.shape[2]
    group_heads = features // head_size
    local_blocks = block_keys.shape[0]
    block_rows = tokens // local_blocks
    score_scale = head_size ** (-0.5)
    ctx_count = lax.axis_size("ctx")
    blocks = local_blocks * ctx_count
    stride = blocks // SUMMARY
    reach = WINDOW - 1
    behind = -(-reach // local_blocks)
    counts = [min(local_blocks, reach - (k - 1) * local_blocks) for k in range(1, behind + 1)]
    span = reach + local_blocks
    n_summary = blocks // stride - 1
    device = lax.axis_index("ctx")
    first_block = device * local_blocks
    low_block = first_block - reach

    incoming = from_behind(next_grad, "section", -1)
    upstream = (head_grad[0].astype(jnp.float32) + incoming[0].astype(jnp.float32)).astype(
        jnp.bfloat16
    )
    products = upstream.astype(jnp.float32) * attn_outputs[0].astype(jnp.float32)
    deltas = jnp.sum(products.reshape(local_blocks, block_rows, group_heads, head_size), axis=3)
    deltas = jnp.swapaxes(deltas, 1, 2)
    lse_rows = jnp.swapaxes(lse_saved[0].reshape(group_heads, local_blocks, block_rows), 0, 1)

    paired = jnp.concatenate([attn_keys[0], attn_values[0]], axis=1)
    own_blocks = paired.reshape(local_blocks, block_rows, 2 * head_size)
    owners = [(k * stride + stride - 1) // local_blocks for k in range(n_summary)]
    radix = 1
    while radix * radix < ctx_count - owners[0]:
        radix += 1

    def member(position, k):
        return (position >= owners[k]) & (position < owners[k] + radix)

    relays = [x for x in range(ctx_count) if any(o <= x < o + radix for o in owners)]
    is_owner = functools.reduce(jnp.logical_or, [device == o for o in owners])
    owned = jnp.where(is_owner, own_blocks[(stride - 1) % local_blocks], 0).astype(jnp.bfloat16)
    held = owned
    pieces = []
    for k in range(behind, 0, -1):
        size = counts[k - 1] * block_rows
        piece = paired[tokens - size :]
        if k < radix:
            arrived = from_behind(jnp.concatenate([piece, owned], axis=0), "ctx", k)
            pieces.append(arrived[:size])
            held = held + arrived[size:]
        else:
            pieces.append(from_behind(piece, "ctx", k))
    pieces.append(paired)
    for shift in range(behind + 1, radix):
        route = [(o, o + shift) for o in owners if o + shift < ctx_count]
        held = held + lax.ppermute(owned, "ctx", route)
    summary_parts = [jnp.where(member(device, k), held, 0) for k in range(n_summary)]
    for hop in range(1, radix):
        shift = hop * radix
        route = [(x, x + shift) for x in relays if x + shift < ctx_count]
        arrived = lax.ppermute(held, "ctx", route)
        for k in range(n_summary):
            summary_parts[k] = summary_parts[k] + jnp.where(member(device - shift, k), arrived, 0)
    summary_kv = jnp.stack(summary_parts).astype(jnp.bfloat16)
    local_table = jnp.concatenate(pieces, axis=0)
    summary_table = summary_kv.reshape(n_summary * block_rows, -1)
    slots = span + n_summary

    targets = block_keys
    slot_of = jnp.where(targets >= low_block, targets - low_block, span + targets // stride)
    slot_of = jnp.where(targets >= 0, slot_of, -1)
    chosen = jnp.any(slot_of[:, :, None] == jnp.arange(slots)[None, None, :], axis=1)
    table_ids = jnp.concatenate(
        [
            low_block + jnp.arange(span, dtype=jnp.int32),
            jnp.arange(n_summary, dtype=jnp.int32) * stride + stride - 1,
        ]
    )
    query_ids = first_block + jnp.arange(local_blocks, dtype=jnp.int32)
    positions = jnp.arange(block_rows, dtype=jnp.int32)
    causal = positions[None, :] <= positions[:, None]
    earlier = table_ids[None, :] < query_ids[:, None]
    allowed = chosen[:, None, :, None] & (earlier[:, None, :, None] | causal[None, :, None, :])

    query_heads = queries[0].reshape(local_blocks, block_rows, group_heads, head_size)
    upstream_heads = upstream.reshape(local_blocks, block_rows, group_heads, head_size)

    def attend(table, mask):
        key_table = table[:, :head_size]
        value_table = table[:, head_size:]
        mask = mask.reshape(local_blocks, block_rows, -1)
        scores = (
            jnp.einsum(
                "rtgh,uh->rgtu", query_heads, key_table, preferred_element_type=jnp.float32
            )
            * score_scale
        )
        weights = jnp.where(mask[:, None], jnp.exp(scores - lse_rows[:, :, :, None]), 0.0)
        dweights = jnp.einsum(
            "rtgh,uh->rgtu", upstream_heads, value_table, preferred_element_type=jnp.float32
        )
        dscores = weights * (dweights - deltas[:, :, :, None])
        weights_low = weights.astype(jnp.bfloat16)
        dscores_low = dscores.astype(jnp.bfloat16)
        grad_q = jnp.einsum(
            "rgtu,uh->rtgh", dscores_low, key_table, preferred_element_type=jnp.float32
        )
        key_part = (
            jnp.einsum(
                "rgtu,rtgh->uh", dscores_low, query_heads, preferred_element_type=jnp.float32
            )
            * score_scale
        )
        value_part = jnp.einsum(
            "rgtu,rtgh->uh", weights_low, upstream_heads, preferred_element_type=jnp.float32
        )
        return grad_q, jnp.concatenate([key_part, value_part], axis=1).astype(jnp.bfloat16)

    grad_local, partial_local = attend(local_table, allowed[:, :, :span])
    grad_summary, summary_partial = attend(summary_table, allowed[:, :, span:])
    grad_q = grad_local + grad_summary
    query_grads = (grad_q * score_scale).reshape(tokens, features).astype(jnp.bfloat16)
    partial = jnp.concatenate([partial_local, summary_partial], axis=0)

    totals = partial[(span - local_blocks) * block_rows : span * block_rows].astype(jnp.float32)
    offset = 0
    for k in range(behind, 0, -1):
        size = counts[k - 1] * block_rows
        returned = from_behind(partial[offset : offset + size], "ctx", -k).astype(jnp.float32)
        totals = totals.at[tokens - size :].add(returned)
        offset += size
    summary_low = partial[span * block_rows :].reshape(n_summary, block_rows, -1)

    def slot_at(position):
        return sum(jnp.where(member(position, k), k, 0) for k in range(n_summary))

    gathered = lax.dynamic_index_in_dim(summary_low, slot_at(device), 0, keepdims=False)
    gathered = gathered.astype(jnp.float32)
    for hop in range(1, radix):
        shift = hop * radix
        route = [(x + shift, x) for x in relays if x + shift < ctx_count]
        outgoing = lax.dynamic_index_in_dim(summary_low, slot_at(device - shift), 0, keepdims=False)
        gathered = gathered + lax.ppermute(outgoing, "ctx", route).astype(jnp.float32)
    owner_total = gathered
    for shift in range(1, radix):
        route = [(o + shift, o) for o in owners if o + shift < ctx_count]
        owner_total = owner_total + lax.ppermute(gathered, "ctx", route)
    start = ((stride - 1) % local_blocks) * block_rows
    mine = jnp.where(is_owner, owner_total, 0.0)
    totals = totals.at[start : start + block_rows].add(mine)
    key_grads = totals[:, :head_size].astype(jnp.bfloat16)
    value_grads = totals[:, head_size:].astype(jnp.bfloat16)
    return (query_grads[None], key_grads[None], value_grads[None])


def solution(mesh):
    placed = (
        P("section", "ctx", None),
        P("section", "ctx", None),
        P("section", "ctx", None),
        P("section", "ctx", None),
        P("section", "ctx", None),
        P("section", "ctx", None),
        P("section", None, "ctx"),
        P("ctx", None),
    )
    return jax.shard_map(
        on_device,
        mesh=mesh,
        in_specs=placed,
        out_specs=(P("section", "ctx", None), P("section", "ctx", None), P("section", "ctx", None)),
        check_vma=False,
    )
```

```python
import functools

import jax
import jax.numpy as jnp
from jax import lax
from jax.sharding import PartitionSpec as P

SUMMARY = 4
WINDOW = 4


def from_behind(block, axis, distance):
    devices = range(lax.axis_size(axis))
    route = [(i - distance, i) for i in devices if i - distance in devices]
    return lax.ppermute(block, axis, route)


def on_device(
    queries, attn_keys, attn_values, attn_outputs, head_grad, next_grad, lse_saved, block_keys
):
    tokens = queries.shape[1]
    features = queries.shape[2]
    head_size = attn_keys.shape[2]
    group_heads = features // head_size
    local_blocks = block_keys.shape[0]
    block_rows = tokens // local_blocks
    score_scale = head_size ** (-0.5)
    ctx_count = lax.axis_size("ctx")
    blocks = local_blocks * ctx_count
    stride = blocks // SUMMARY
    reach = WINDOW - 1
    behind = -(-reach // local_blocks)
    counts = [min(local_blocks, reach - (k - 1) * local_blocks) for k in range(1, behind + 1)]
    span = reach + local_blocks
    n_summary = blocks // stride - 1
    device = lax.axis_index("ctx")
    first_block = device * local_blocks
    low_block = first_block - reach

    incoming = from_behind(next_grad, "section", -1)
    upstream = (head_grad[0].astype(jnp.float32) + incoming[0].astype(jnp.float32)).astype(
        jnp.bfloat16
    )
    products = upstream.astype(jnp.float32) * attn_outputs[0].astype(jnp.float32)
    deltas = jnp.sum(products.reshape(local_blocks, block_rows, group_heads, head_size), axis=3)
    deltas = jnp.swapaxes(deltas, 1, 2)
    lse_rows = jnp.swapaxes(lse_saved[0].reshape(group_heads, local_blocks, block_rows), 0, 1)

    paired = jnp.concatenate([attn_keys[0], attn_values[0]], axis=1)
    own_blocks = paired.reshape(local_blocks, block_rows, 2 * head_size)
    owners = [(k * stride + stride - 1) // local_blocks for k in range(n_summary)]
    radix = 1
    while radix * radix < ctx_count - owners[0]:
        radix += 1

    def member(position, k):
        return (position >= owners[k]) & (position < owners[k] + radix)

    relays = [x for x in range(ctx_count) if any(o <= x < o + radix for o in owners)]
    is_owner = functools.reduce(jnp.logical_or, [device == o for o in owners])
    owned = jnp.where(is_owner, own_blocks[(stride - 1) % local_blocks], 0).astype(jnp.bfloat16)
    held = owned
    pieces = []
    for k in range(behind, 0, -1):
        size = counts[k - 1] * block_rows
        piece = paired[tokens - size :]
        if k < radix:
            arrived = from_behind(jnp.concatenate([piece, owned], axis=0), "ctx", k)
            pieces.append(arrived[:size])
            held = held + arrived[size:]
        else:
            pieces.append(from_behind(piece, "ctx", k))
    pieces.append(paired)
    for shift in range(behind + 1, radix):
        route = [(o, o + shift) for o in owners if o + shift < ctx_count]
        held = held + lax.ppermute(owned, "ctx", route)
    summary_parts = [jnp.where(member(device, k), held, 0) for k in range(n_summary)]
    for hop in range(1, radix):
        shift = hop * radix
        route = [(x, x + shift) for x in relays if x + shift < ctx_count]
        arrived = lax.ppermute(held, "ctx", route)
        for k in range(n_summary):
            summary_parts[k] = summary_parts[k] + jnp.where(member(device - shift, k), arrived, 0)
    summary_kv = jnp.stack(summary_parts).astype(jnp.bfloat16)
    local_table = jnp.concatenate(pieces, axis=0)
    summary_table = summary_kv.reshape(n_summary * block_rows, -1)
    slots = span + n_summary

    targets = block_keys
    slot_of = jnp.where(targets >= low_block, targets - low_block, span + targets // stride)
    slot_of = jnp.where(targets >= 0, slot_of, -1)
    chosen = jnp.any(slot_of[:, :, None] == jnp.arange(slots)[None, None, :], axis=1)
    table_ids = jnp.concatenate(
        [
            low_block + jnp.arange(span, dtype=jnp.int32),
            jnp.arange(n_summary, dtype=jnp.int32) * stride + stride - 1,
        ]
    )
    query_ids = first_block + jnp.arange(local_blocks, dtype=jnp.int32)
    positions = jnp.arange(block_rows, dtype=jnp.int32)
    causal = positions[None, :] <= positions[:, None]
    earlier = table_ids[None, :] < query_ids[:, None]
    allowed = chosen[:, None, :, None] & (earlier[:, None, :, None] | causal[None, :, None, :])

    query_heads = queries[0].reshape(local_blocks, block_rows, group_heads, head_size)
    upstream_heads = upstream.reshape(local_blocks, block_rows, group_heads, head_size)

    def attend(table, mask):
        key_table = table[:, :head_size]
        value_table = table[:, head_size:]
        mask = mask.reshape(local_blocks, block_rows, -1)
        scores = (
            jnp.einsum(
                "rtgh,uh->rgtu", query_heads, key_table, preferred_element_type=jnp.float32
            )
            * score_scale
        )
        weights = jnp.where(mask[:, None], jnp.exp(scores - lse_rows[:, :, :, None]), 0.0)
        dweights = jnp.einsum(
            "rtgh,uh->rgtu", upstream_heads, value_table, preferred_element_type=jnp.float32
        )
        dscores = weights * (dweights - deltas[:, :, :, None])
        weights_low = weights.astype(jnp.bfloat16)
        dscores_low = dscores.astype(jnp.bfloat16)
        grad_q = jnp.einsum(
            "rgtu,uh->rtgh", dscores_low, key_table, preferred_element_type=jnp.float32
        )
        key_part = (
            jnp.einsum(
                "rgtu,rtgh->uh", dscores_low, query_heads, preferred_element_type=jnp.float32
            )
            * score_scale
        )
        value_part = jnp.einsum(
            "rgtu,rtgh->uh", weights_low, upstream_heads, preferred_element_type=jnp.float32
        )
        return grad_q, jnp.concatenate([key_part, value_part], axis=1).astype(jnp.bfloat16)

    grad_local, partial_local = attend(local_table, allowed[:, :, :span])
    grad_summary, summary_partial = attend(summary_table, allowed[:, :, span:])
    grad_q = grad_local + grad_summary
    query_grads = (grad_q * score_scale).reshape(tokens, features).astype(jnp.bfloat16)
    partial = jnp.concatenate([partial_local, summary_partial], axis=0)

    totals = partial[(span - local_blocks) * block_rows : span * block_rows].astype(jnp.float32)
    summary_low = partial[span * block_rows :].reshape(n_summary, block_rows, -1)

    def slot_at(position):
        return sum(jnp.where(member(position, k), k, 0) for k in range(n_summary))

    gathered = lax.dynamic_index_in_dim(summary_low, slot_at(device), 0, keepdims=False)
    gathered = gathered.astype(jnp.float32)
    for hop in range(1, radix):
        shift = hop * radix
        route = [(x + shift, x) for x in relays if x + shift < ctx_count]
        outgoing = lax.dynamic_index_in_dim(summary_low, slot_at(device - shift), 0, keepdims=False)
        gathered = gathered + lax.ppermute(outgoing, "ctx", route).astype(jnp.float32)
    owner_total = gathered
    offset = 0
    for k in range(behind, 0, -1):
        size = counts[k - 1] * block_rows
        piece = partial[offset : offset + size].astype(jnp.float32)
        if k < radix:
            returned = from_behind(jnp.concatenate([piece, gathered], axis=0), "ctx", -k)
            owner_total = owner_total + returned[size:]
            returned = returned[:size]
        else:
            returned = from_behind(piece, "ctx", -k)
        totals = totals.at[tokens - size :].add(returned)
        offset += size
    for shift in range(behind + 1, radix):
        route = [(o + shift, o) for o in owners if o + shift < ctx_count]
        owner_total = owner_total + lax.ppermute(gathered, "ctx", route)
    start = ((stride - 1) % local_blocks) * block_rows
    mine = jnp.where(is_owner, owner_total, 0.0)
    totals = totals.at[start : start + block_rows].add(mine)
    key_grads = totals[:, :head_size].astype(jnp.bfloat16)
    value_grads = totals[:, head_size:].astype(jnp.bfloat16)
    return (query_grads[None], key_grads[None], value_grads[None])


def solution(mesh):
    placed = (
        P("section", "ctx", None),
        P("section", "ctx", None),
        P("section", "ctx", None),
        P("section", "ctx", None),
        P("section", "ctx", None),
        P("section", "ctx", None),
        P("section", None, "ctx"),
        P("ctx", None),
    )
    return jax.shard_map(
        on_device,
        mesh=mesh,
        in_specs=placed,
        out_specs=(P("section", "ctx", None), P("section", "ctx", None), P("section", "ctx", None)),
        check_vma=False,
    )
```

```python
import functools

import jax
import jax.numpy as jnp
from jax import lax
from jax.sharding import PartitionSpec as P

SUMMARY = 4
WINDOW = 4


def from_behind(block, axis, distance):
    devices = range(lax.axis_size(axis))
    route = [(i - distance, i) for i in devices if i - distance in devices]
    return lax.ppermute(block, axis, route)


def on_device(
    queries, attn_keys, attn_values, attn_outputs, head_grad, next_grad, lse_saved, block_keys
):
    tokens = queries.shape[1]
    features = queries.shape[2]
    head_size = attn_keys.shape[2]
    group_heads = features // head_size
    local_blocks = block_keys.shape[0]
    block_rows = tokens // local_blocks
    score_scale = head_size ** (-0.5)
    ctx_count = lax.axis_size("ctx")
    blocks = local_blocks * ctx_count
    stride = blocks // SUMMARY
    reach = WINDOW - 1
    behind = -(-reach // local_blocks)
    counts = [min(local_blocks, reach - (k - 1) * local_blocks) for k in range(1, behind + 1)]
    span = reach + local_blocks
    n_summary = blocks // stride - 1
    device = lax.axis_index("ctx")
    first_block = device * local_blocks
    low_block = first_block - reach

    incoming = from_behind(next_grad, "section", -1)
    upstream = (head_grad[0].astype(jnp.float32) + incoming[0].astype(jnp.float32)).astype(
        jnp.bfloat16
    )
    products = upstream.astype(jnp.float32) * attn_outputs[0].astype(jnp.float32)
    deltas = jnp.sum(products.reshape(local_blocks, block_rows, group_heads, head_size), axis=3)
    deltas = jnp.swapaxes(deltas, 1, 2)
    lse_rows = jnp.swapaxes(lse_saved[0].reshape(group_heads, local_blocks, block_rows), 0, 1)

    paired = jnp.concatenate([attn_keys[0], attn_values[0]], axis=1)
    own_blocks = paired.reshape(local_blocks, block_rows, 2 * head_size)
    owners = [(k * stride + stride - 1) // local_blocks for k in range(n_summary)]
    radix = 1
    while radix * radix < ctx_count - owners[0]:
        radix += 1

    def member(position, k):
        return (position >= owners[k]) & (position < owners[k] + radix)

    relays = [x for x in range(ctx_count) if any(o <= x < o + radix for o in owners)]
    is_owner = functools.reduce(jnp.logical_or, [device == o for o in owners])
    owned = jnp.where(is_owner, own_blocks[(stride - 1) % local_blocks], 0).astype(jnp.bfloat16)
    held = owned
    pieces = []
    for k in range(behind, 0, -1):
        size = counts[k - 1] * block_rows
        piece = paired[tokens - size :]
        if k < radix:
            arrived = from_behind(jnp.concatenate([piece, owned], axis=0), "ctx", k)
            pieces.append(arrived[:size])
            held = held + arrived[size:]
        else:
            pieces.append(from_behind(piece, "ctx", k))
    pieces.append(paired)
    for shift in range(behind + 1, radix):
        route = [(o, o + shift) for o in owners if o + shift < ctx_count]
        held = held + lax.ppermute(owned, "ctx", route)
    summary_parts = [jnp.where(member(device, k), held, 0) for k in range(n_summary)]
    for hop in range(1, radix):
        shift = hop * radix
        route = [(x, x + shift) for x in relays if x + shift < ctx_count]
        arrived = lax.ppermute(held, "ctx", route)
        for k in range(n_summary):
            summary_parts[k] = summary_parts[k] + jnp.where(member(device - shift, k), arrived, 0)
    summary_kv = jnp.stack(summary_parts).astype(jnp.bfloat16)
    local_table = jnp.concatenate(pieces, axis=0)
    summary_table = summary_kv.reshape(n_summary * block_rows, -1)
    slots = span + n_summary

    targets = block_keys
    slot_of = jnp.where(targets >= low_block, targets - low_block, span + targets // stride)
    slot_of = jnp.where(targets >= 0, slot_of, -1)
    chosen = jnp.any(slot_of[:, :, None] == jnp.arange(slots)[None, None, :], axis=1)
    table_ids = jnp.concatenate(
        [
            low_block + jnp.arange(span, dtype=jnp.int32),
            jnp.arange(n_summary, dtype=jnp.int32) * stride + stride - 1,
        ]
    )
    query_ids = first_block + jnp.arange(local_blocks, dtype=jnp.int32)
    positions = jnp.arange(block_rows, dtype=jnp.int32)
    causal = positions[None, :] <= positions[:, None]
    earlier = table_ids[None, :] < query_ids[:, None]
    allowed = chosen[:, None, :, None] & (earlier[:, None, :, None] | causal[None, :, None, :])

    query_heads = queries[0].reshape(local_blocks, block_rows, group_heads, head_size)
    upstream_heads = upstream.reshape(local_blocks, block_rows, group_heads, head_size)

    def attend(table, mask):
        key_table = table[:, :head_size]
        value_table = table[:, head_size:]
        mask = mask.reshape(local_blocks, block_rows, -1)
        scores = (
            jnp.einsum(
                "rtgh,uh->rgtu", query_heads, key_table, preferred_element_type=jnp.float32
            )
            * score_scale
        )
        weights = jnp.where(mask[:, None], jnp.exp(scores - lse_rows[:, :, :, None]), 0.0)
        dweights = jnp.einsum(
            "rtgh,uh->rgtu", upstream_heads, value_table, preferred_element_type=jnp.float32
        )
        dscores = weights * (dweights - deltas[:, :, :, None])
        weights_low = weights.astype(jnp.bfloat16)
        dscores_low = dscores.astype(jnp.bfloat16)
        grad_q = jnp.einsum(
            "rgtu,uh->rtgh", dscores_low, key_table, preferred_element_type=jnp.float32
        )
        key_part = (
            jnp.einsum(
                "rgtu,rtgh->uh", dscores_low, query_heads, preferred_element_type=jnp.float32
            )
            * score_scale
        )
        value_part = jnp.einsum(
            "rgtu,rtgh->uh", weights_low, upstream_heads, preferred_element_type=jnp.float32
        )
        return grad_q, jnp.concatenate([key_part, value_part], axis=1).astype(jnp.bfloat16)

    grad_local, partial_local = attend(local_table, allowed[:, :, :span])
    grad_summary, summary_partial = attend(summary_table, allowed[:, :, span:])
    grad_q = grad_local + grad_summary
    query_grads = (grad_q * score_scale).reshape(tokens, features).astype(jnp.bfloat16)
    partial = jnp.concatenate([partial_local, summary_partial], axis=0)

    totals = partial[(span - local_blocks) * block_rows : span * block_rows].astype(jnp.float32)
    offset = 0
    for k in range(behind, 0, -1):
        size = counts[k - 1] * block_rows
        returned = from_behind(partial[offset : offset + size], "ctx", -k).astype(jnp.float32)
        totals = totals.at[tokens - size :].add(returned)
        offset += size
    summary_low = partial[span * block_rows :].reshape(n_summary, block_rows, -1)

    def slot_at(position):
        picked = [jnp.where(member(position, k), summary_low[k], 0) for k in range(n_summary)]
        return functools.reduce(jnp.add, picked).astype(jnp.bfloat16)

    gathered = slot_at(device).astype(jnp.float32)
    for hop in range(1, radix):
        shift = hop * radix
        route = [(x + shift, x) for x in relays if x + shift < ctx_count]
        outgoing = slot_at(device - shift)
        gathered = gathered + lax.ppermute(outgoing, "ctx", route).astype(jnp.float32)
    owner_total = gathered
    for shift in range(1, radix):
        route = [(o + shift, o) for o in owners if o + shift < ctx_count]
        owner_total = owner_total + lax.ppermute(gathered, "ctx", route)
    start = ((stride - 1) % local_blocks) * block_rows
    mine = jnp.where(is_owner, owner_total, 0.0)
    totals = totals.at[start : start + block_rows].add(mine)
    key_grads = totals[:, :head_size].astype(jnp.bfloat16)
    value_grads = totals[:, head_size:].astype(jnp.bfloat16)
    return (query_grads[None], key_grads[None], value_grads[None])


def solution(mesh):
    placed = (
        P("section", "ctx", None),
        P("section", "ctx", None),
        P("section", "ctx", None),
        P("section", "ctx", None),
        P("section", "ctx", None),
        P("section", "ctx", None),
        P("section", None, "ctx"),
        P("ctx", None),
    )
    return jax.shard_map(
        on_device,
        mesh=mesh,
        in_specs=placed,
        out_specs=(P("section", "ctx", None), P("section", "ctx", None), P("section", "ctx", None)),
        check_vma=False,
    )
```
